256 devices in a mesh: row: 32 (over y, z_lo, core), col: 8 (over z_hi, x).
Axes of the slice: x: 4, y: 4, z: 8 (z_hi: 2, z_lo: 4; z = z_hi * 4 + z_lo), core: 2. Of those that a mesh axis runs over, the one named last changes fastest.
Arguments:
- cells: bfloat16 [1024, 4096, 128], P('row', 'col'), may hold values from -6 to 6
- upstream: bfloat16 [1024, 4096, 128], P('row', 'col'), may hold values from -6 to 6
- counts: int32 [1024], P('row'), may hold values from 1 to 4096, as said below
- key_weight: bfloat16 [128, 128], replicated, may hold values from -0.5 to 0.5
- value_weight: bfloat16 [128, 128], replicated, may hold values from -0.5 to 0.5
- out_weight: bfloat16 [128, 128], replicated, may hold values from -0.5 to 0.5
- row_query: float32 [128], replicated, may hold values from -60 to 60
- col_query: float32 [128], replicated, may hold values from -60 to 60
Outputs:
- cell_grad: bfloat16 [1024, 4096, 128], P('row', 'col')
- key_weight_grad: float32 [128, 128], replicated
- value_weight_grad: float32 [128, 128], replicated
- out_weight_grad: float32 [128, 128], replicated
- row_query_grad: float32 [128], replicated
- col_query_grad: float32 [128], replicated
The draws below stay inside these ranges and needn't reach their ends.
Inputs may be any that keep to these rules, and one draw needn't show every extreme that they name: `counts`: some row uses all 4096 columns and some row uses exactly one.
All inputs are finite; a program needn't handle non-finite values.
Results may differ from the reference program's by a relative error of at most 0.0047.
Values sent between devices are 32-bit elements; how exact they have to be, the bound alone decides.
No kernel may reach another device: no remote copies, remote signals or barrier semaphores. Data moves between devices by JAX's collectives and lax.ppermute only.
A program may use at most 192 MiB of HBM per device.

```python
import math
import jax
import jax.numpy as jnp
from jax import lax

H = 128
RD = 32
R = 1024
C = 4096


def query_vector(key):
    base = jnp.clip(jax.random.normal(key, (H,), jnp.float32), -4.0, 4.0)
    return base


def draw_row_query(key, part):
    return query_vector(jax.random.fold_in(key, 11))


def draw_col_query(key, part):
    return query_vector(jax.random.fold_in(key, 23))


def draw_counts(key, part):
    key_a = jax.random.fold_in(key, 1)
    key_b = jax.random.fold_in(key, 2)
    key_c = jax.random.fold_in(key, 3)
    key_d = jax.random.fold_in(key, 4)
    first_len = jax.random.randint(key_a, (R,), 1, C + 1, jnp.int32)
    second_len = jax.random.randint(key_b, (R,), 1, C + 1, jnp.int32)
    lengths = jnp.minimum(first_len, second_len)
    full_row = jax.random.randint(key_c, (), 0, R, jnp.int32)
    short_row = (full_row + 1 + jax.random.randint(key_d, (), 0, R - 1, jnp.int32)) % R
    row_ids = jnp.arange(R, dtype=jnp.int32)
    lengths = jnp.where(row_ids == full_row, C, lengths)
    lengths = jnp.where(row_ids == short_row, 1, lengths)
    return lengths.astype(jnp.int32)


def steps_of(key, extent, cuts, least, high):
    loudness = 1.0
    for axis_at, parts in cuts:
        draws = jax.random.uniform(jax.random.fold_in(jax.random.fold_in(key, 6), axis_at), (parts,), jnp.float32, least / len(cuts), high / len(cuts))
        loudness = loudness * jnp.repeat(jnp.exp(draws), extent[axis_at] // parts).reshape((-1,) + (1,) * (len(extent) - 1 - axis_at))
    return loudness


def centred(rng, shape, spread, limit, pieces=(), held_as=jnp.bfloat16):
    level = steps_of(rng, shape, pieces, -0.22, 0.18) if pieces else 1.0
    values = jax.random.normal(rng, shape, jnp.float32) * spread * level
    return jnp.minimum(jnp.maximum(values, -limit), limit).astype(held_as)


def setup_inputs(seed: int = 0) -> dict:
    keys = jax.random.split(jax.random.key(seed), 9)
    return {
        "cells": centred(keys[0], (R, C, H), 1.0, 6.0, ((0, 32), (1, 8))),
        "upstream": centred(keys[1], (R, C, H), 1.0, 6.0, ((0, 32), (1, 8))),
        "counts": draw_counts(jax.random.fold_in(keys[8], 71), 0),
        "key_weight": centred(keys[3], (H, H), H ** -0.5, 0.5),
        "value_weight": centred(keys[4], (H, H), H ** -0.5, 0.5),
        "out_weight": centred(keys[5], (H, H), H ** -0.5, 0.5),
        "row_query": draw_row_query(jax.random.fold_in(keys[8], 71), 0),
        "col_query": draw_col_query(jax.random.fold_in(keys[8], 71), 0),
    }


NEG_FILL = -1e+30
HIGH = lax.Precision.HIGHEST

def project(block_cells, key_weight, value_weight, row_query, col_query, score_scale):
    shape = block_cells.shape
    flat_cells = block_cells.reshape(-1, shape[-1])
    key_rows = jnp.dot(flat_cells, key_weight, preferred_element_type=jnp.float32).reshape(shape)
    values = jnp.dot(flat_cells, value_weight, preferred_element_type=jnp.float32).reshape(shape)
    row_score = jnp.einsum('rch,h->rc', key_rows, row_query, precision=HIGH) * score_scale
    col_score = jnp.einsum('rch,h->rc', key_rows, col_query, precision=HIGH) * score_scale
    return (key_rows, values, row_score, col_score)

def reference(cells, upstream, counts, key_weight, value_weight, out_weight, row_query, col_query):
    score_scale = 1.0 / math.sqrt(H)
    block_count = R // RD
    cell_blocks = cells.reshape(block_count, RD, C, H)
    upstream_blocks = upstream.reshape(block_count, RD, C, H)
    count_blocks = counts.reshape(block_count, RD)
    column_ids = jnp.arange(C, dtype=jnp.int32)

    def first_pass(carry, block):
        col_max, col_total, col_pooled, col_cot = carry
        block_cells, block_up, block_counts = block
        key_rows, values, row_score, col_score = project(block_cells, key_weight, value_weight, row_query, col_query, score_scale)
        live_mask = column_ids[None, :] < block_counts[:, None]
        row_max = lax.optimization_barrier(jnp.max(jnp.where(live_mask, row_score, NEG_FILL), 1))
        row_weights = jnp.where(live_mask, jnp.exp(row_score - row_max[:, None]), 0.0)
        row_total = lax.optimization_barrier(jnp.sum(row_weights, 1))
        row_pooled = jnp.einsum('rc,rch->rh', row_weights, values, precision=HIGH)
        block_max = lax.optimization_barrier(jnp.max(jnp.where(live_mask, col_score, NEG_FILL), 0))
        joint_max = jnp.maximum(col_max, block_max)
        decay = jnp.exp(col_max - joint_max)
        col_weights = jnp.where(live_mask, jnp.exp(col_score - joint_max[None, :]), 0.0)
        col_total = col_total * decay + lax.optimization_barrier(jnp.sum(col_weights, 0))
        col_pooled = col_pooled * decay[:, None] + jnp.einsum('rc,rch->ch', col_weights, values, precision=HIGH)
        block_up_f = block_up.astype(jnp.float32)
        col_cot = col_cot + lax.optimization_barrier(jnp.sum(block_up_f, 0))
        row_cot = lax.optimization_barrier(jnp.sum(block_up_f, 1))
        return ((joint_max, col_total, col_pooled, col_cot), (row_max, row_total, row_pooled / row_total[:, None], row_cot))
    start = (jnp.full((C,), NEG_FILL, jnp.float32), jnp.zeros((C,), jnp.float32), jnp.zeros((C, H), jnp.float32), jnp.zeros((C, H), jnp.float32))
    (col_max, col_total, col_pooled, col_cot), row_parts = lax.scan(first_pass, start, (cell_blocks, upstream_blocks, count_blocks))
    col_hub = col_pooled / col_total[:, None]
    out_t = out_weight.astype(jnp.float32).T
    col_grad = jnp.dot(col_cot, out_t, precision=HIGH)
    col_dot = lax.optimization_barrier(jnp.sum(col_hub * col_grad, -1))

    def second_pass(carry, block):
        grad_key, grad_value, grad_out, grad_rq, grad_cq = carry
        block_cells, block_up, block_counts, row_max, row_total, row_hub, row_cot = block
        key_rows, values, row_score, col_score = project(block_cells, key_weight, value_weight, row_query, col_query, score_scale)
        live_mask = column_ids[None, :] < block_counts[:, None]
        row_prob = jnp.where(live_mask, jnp.exp(row_score - row_max[:, None]), 0.0) / row_total[:, None]
        col_prob = jnp.where(live_mask, jnp.exp(col_score - col_max[None, :]), 0.0) / col_total[None, :]
        row_grad = jnp.dot(row_cot, out_t, precision=HIGH)
        row_dot = lax.optimization_barrier(jnp.sum(row_hub * row_grad, -1))
        row_dp = jnp.einsum('rch,rh->rc', values, row_grad, precision=HIGH)
        col_dp = jnp.einsum('rch,ch->rc', values, col_grad, precision=HIGH)
        row_ds = row_prob * (row_dp - row_dot[:, None])
        col_ds = col_prob * (col_dp - col_dot[None, :])
        value_grad = (row_prob[..., None] * row_grad[:, None, :] + col_prob[..., None] * col_grad[None, :, :]).astype(jnp.bfloat16)
        key_grad = ((row_ds[..., None] * row_query + col_ds[..., None] * col_query) * score_scale).astype(jnp.bfloat16)
        grad_rq = grad_rq + jnp.einsum('rc,rch->h', row_ds, key_rows, precision=HIGH) * score_scale
        grad_cq = grad_cq + jnp.einsum('rc,rch->h', col_ds, key_rows, precision=HIGH) * score_scale
        flat_cells = block_cells.reshape(-1, H)
        flat_kg = key_grad.reshape(-1, H)
        flat_vg = value_grad.reshape(-1, H)
        grad_key = grad_key + jnp.einsum('nh,nk->hk', flat_cells, flat_kg, preferred_element_type=jnp.float32)
        grad_value = grad_value + jnp.einsum('nh,nk->hk', flat_cells, flat_vg, preferred_element_type=jnp.float32)
        grad_out = grad_out + jnp.einsum('rh,rk->hk', row_hub, row_cot, precision=HIGH)
        back = jnp.einsum('nk,hk->nh', flat_kg, key_weight, preferred_element_type=jnp.float32)
        back = back + jnp.einsum('nk,hk->nh', flat_vg, value_weight, preferred_element_type=jnp.float32)
        cell_block = (block_up.astype(jnp.float32) + back.reshape(block_up.shape)).astype(jnp.bfloat16)
        return ((grad_key, grad_value, grad_out, grad_rq, grad_cq), cell_block)
    zero_mat = jnp.zeros((H, H), jnp.float32)
    zero_vec = jnp.zeros((H,), jnp.float32)
    row_max, row_total, row_hub, row_cot = row_parts
    (grad_key, grad_value, grad_out, grad_rq, grad_cq), cell_blocks_out = lax.scan(second_pass, (zero_mat, zero_mat, zero_mat, zero_vec, zero_vec), (cell_blocks, upstream_blocks, count_blocks, row_max, row_total, row_hub, row_cot))
    grad_out = grad_out + jnp.einsum('ch,ck->hk', col_hub, col_cot, precision=HIGH)
    return (cell_blocks_out.reshape(R, C, H), grad_key, grad_value, grad_out, grad_rq, grad_cq)
```

```python
import math

import jax
import jax.numpy as jnp
from jax import lax
from jax.sharding import PartitionSpec as P

NEG_FILL = -1e30
HIGH = lax.Precision.HIGHEST


def butterfly(state, axis, combine):
    size = lax.axis_size(axis)
    me = lax.axis_index(axis)
    step = 1
    while step < size:
        other = lax.ppermute(state, axis, [(i, i ^ step) for i in range(size)])
        upper = (me & step) != 0
        low = jax.tree.map(lambda a, b: jnp.where(upper, b, a), state, other)
        high = jax.tree.map(lambda a, b: jnp.where(upper, a, b), state, other)
        state = combine(low, high)
        step *= 2
    return state


def add_tree(a, b):
    return jax.tree.map(jnp.add, a, b)


def softmax_merge(a, b):
    max_a, total_a, pooled_a = a
    max_b, total_b, pooled_b = b
    joint = jnp.maximum(max_a, max_b)
    scale_a = jnp.exp(max_a - joint)
    scale_b = jnp.exp(max_b - joint)
    total = total_a * scale_a + total_b * scale_b
    pooled = pooled_a * scale_a[:, None] + pooled_b * scale_b[:, None]
    return (joint, total, pooled)


def on_device(cells, upstream, counts, key_weight, value_weight, out_weight, row_query, col_query):
    row_count, col_count, feature_width = cells.shape
    score_scale = 1.0 / math.sqrt(feature_width)
    upstream_f = upstream.astype(jnp.float32)
    local_row_cot = jnp.sum(upstream_f, 1)
    local_col_cot = jnp.sum(upstream_f, 0)
    row_cot = butterfly(local_row_cot, "col", jnp.add)
    col_cot = butterfly(local_col_cot, "row", jnp.add)

    flat_cells = cells.reshape(-1, feature_width)
    key_rows = jnp.dot(flat_cells, key_weight, preferred_element_type=jnp.float32).reshape(
        cells.shape
    )
    values = jnp.dot(flat_cells, value_weight, preferred_element_type=jnp.float32).reshape(
        cells.shape
    )
    row_score = jnp.einsum("rch,h->rc", key_rows, row_query, precision=HIGH) * score_scale
    col_score = jnp.einsum("rch,h->rc", key_rows, col_query, precision=HIGH) * score_scale
    column_ids = lax.axis_index("col") * col_count + jnp.arange(col_count, dtype=jnp.int32)
    live_mask = column_ids[None, :] < counts[:, None]

    row_local_max = jnp.max(jnp.where(live_mask, row_score, NEG_FILL), 1)
    col_local_max = jnp.max(jnp.where(live_mask, col_score, NEG_FILL), 0)
    row_local_w = jnp.where(live_mask, jnp.exp(row_score - row_local_max[:, None]), 0.0)
    col_local_w = jnp.where(live_mask, jnp.exp(col_score - col_local_max[None, :]), 0.0)
    row_state = (
        row_local_max,
        jnp.sum(row_local_w, 1),
        jnp.einsum("rc,rch->rh", row_local_w, values, precision=HIGH),
    )
    col_state = (
        col_local_max,
        jnp.sum(col_local_w, 0),
        jnp.einsum("rc,rch->ch", col_local_w, values, precision=HIGH),
    )
    row_max, row_total, row_pooled = butterfly(row_state, "col", softmax_merge)
    col_max, col_total, col_pooled = butterfly(col_state, "row", softmax_merge)

    row_weights = jnp.where(live_mask, jnp.exp(row_score - row_max[:, None]), 0.0)
    col_weights = jnp.where(live_mask, jnp.exp(col_score - col_max[None, :]), 0.0)
    row_hub = row_pooled / row_total[:, None]
    col_hub = col_pooled / col_total[:, None]
    out_trans = out_weight.astype(jnp.float32).T
    row_grad = jnp.dot(row_cot, out_trans, precision=HIGH)
    col_grad = jnp.dot(col_cot, out_trans, precision=HIGH)
    row_prob = row_weights / row_total[:, None]
    col_prob = col_weights / col_total[None, :]
    row_dot = jnp.sum(row_hub * row_grad, -1)
    col_dot = jnp.sum(col_hub * col_grad, -1)
    row_dp = jnp.einsum("rch,rh->rc", values, row_grad, precision=HIGH)
    col_dp = jnp.einsum("rch,ch->rc", values, col_grad, precision=HIGH)
    row_ds = row_prob * (row_dp - row_dot[:, None])
    col_ds = col_prob * (col_dp - col_dot[None, :])
    value_grad = (
        row_prob[..., None] * row_grad[:, None, :] + col_prob[..., None] * col_grad[None, :, :]
    ).astype(jnp.bfloat16)
    key_grad = (
        (row_ds[..., None] * row_query + col_ds[..., None] * col_query) * score_scale
    ).astype(jnp.bfloat16)
    row_query_part = jnp.einsum("rc,rch->h", row_ds, key_rows, precision=HIGH) * score_scale
    col_query_part = jnp.einsum("rc,rch->h", col_ds, key_rows, precision=HIGH) * score_scale
    flat_kg = key_grad.reshape(-1, feature_width)
    flat_vg = value_grad.reshape(-1, feature_width)
    key_part = jnp.einsum("nh,nk->hk", flat_cells, flat_kg, preferred_element_type=jnp.float32)
    value_part = jnp.einsum("nh,nk->hk", flat_cells, flat_vg, preferred_element_type=jnp.float32)
    out_part = jnp.einsum("rh,rk->hk", row_hub, local_row_cot, precision=HIGH)
    out_part = out_part + jnp.einsum("ch,ck->hk", col_hub, local_col_cot, precision=HIGH)
    packed = jnp.concatenate(
        [key_part, value_part, out_part, row_query_part[None], col_query_part[None]], 0
    )
    packed = butterfly(butterfly(packed, "col", jnp.add), "row", jnp.add)
    key_total = packed[:feature_width]
    value_total = packed[feature_width : 2 * feature_width]
    out_total = packed[2 * feature_width : 3 * feature_width]
    row_query_total = packed[3 * feature_width]
    col_query_total = packed[3 * feature_width + 1]
    back = jnp.einsum("nk,hk->nh", flat_kg, key_weight, preferred_element_type=jnp.float32)
    back = back + jnp.einsum("nk,hk->nh", flat_vg, value_weight, preferred_element_type=jnp.float32)
    cell_grad = (upstream_f + back.reshape(cells.shape)).astype(jnp.bfloat16)
    return (cell_grad, key_total, value_total, out_total, row_query_total, col_query_total)


def solution(mesh):
    placed = (P("row", "col", None), P("row", "col", None), P("row"), P(), P(), P(), P(), P())
    return jax.shard_map(
        on_device,
        mesh=mesh,
        in_specs=placed,
        out_specs=(P("row", "col", None), P(), P(), P(), P(), P()),
        check_vma=False,
    )
```

```python
import math

import jax
import jax.numpy as jnp
from jax import lax
from jax.sharding import PartitionSpec as P

NEG_FILL = -1e30
HIGH = lax.Precision.HIGHEST
LANES = 128


def butterfly(state, axis, combine):
    size = lax.axis_size(axis)
    me = lax.axis_index(axis)
    step = 1
    while step < size:
        other = lax.ppermute(state, axis, [(i, i ^ step) for i in range(size)])
        upper = (me & step) != 0
        low = jnp.where(upper, other, state)
        high = jnp.where(upper, state, other)
        state = combine(low, high)
        step *= 2
    return state


def vec_rows(vec):
    pad = (-vec.shape[0]) % LANES
    return jnp.pad(vec, (0, pad)).reshape(-1, LANES)


def pack_hub(local_max, local_total, pooled, cot):
    return jnp.concatenate([pooled, cot, vec_rows(local_max), vec_rows(local_total)], 0)


def unpack_hub(packed, count):
    extra = -(-count // LANES)
    pooled = packed[:count]
    cot = packed[count : 2 * count]
    hub_max = packed[2 * count : 2 * count + extra].reshape(-1)[:count]
    total = packed[2 * count + extra :].reshape(-1)[:count]
    return hub_max, total, pooled, cot


def hub_merge(count):
    def merge(a, b):
        max_a, total_a, pooled_a, cot_a = unpack_hub(a, count)
        max_b, total_b, pooled_b, cot_b = unpack_hub(b, count)
        joint = jnp.maximum(max_a, max_b)
        scale_a = jnp.exp(max_a - joint)
        scale_b = jnp.exp(max_b - joint)
        total = total_a * scale_a + total_b * scale_b
        pooled = pooled_a * scale_a[:, None] + pooled_b * scale_b[:, None]
        return pack_hub(joint, total, pooled, cot_a + cot_b)

    return merge


def on_device(cells, upstream, counts, key_weight, value_weight, out_weight, row_query, col_query):
    row_count, col_count, feature_width = cells.shape
    score_scale = 1.0 / math.sqrt(feature_width)
    cells_f = cells.astype(jnp.float32)
    upstream_f = upstream.astype(jnp.float32)
    key_f = key_weight.astype(jnp.float32)
    value_f = value_weight.astype(jnp.float32)
    local_row_cot = jnp.sum(upstream_f, 1)
    local_col_cot = jnp.sum(upstream_f, 0)

    row_key_query = jnp.dot(key_f, row_query, precision=HIGH)
    col_key_query = jnp.dot(key_f, col_query, precision=HIGH)
    row_score = jnp.einsum("rch,h->rc", cells_f, row_key_query, precision=HIGH) * score_scale
    col_score = jnp.einsum("rch,h->rc", cells_f, col_key_query, precision=HIGH) * score_scale
    column_ids = lax.axis_index("col") * col_count + jnp.arange(col_count, dtype=jnp.int32)
    live_mask = column_ids[None, :] < counts[:, None]

    row_local_max = jnp.max(jnp.where(live_mask, row_score, NEG_FILL), 1)
    col_local_max = jnp.max(jnp.where(live_mask, col_score, NEG_FILL), 0)
    row_local_w = jnp.where(live_mask, jnp.exp(row_score - row_local_max[:, None]), 0.0)
    col_local_w = jnp.where(live_mask, jnp.exp(col_score - col_local_max[None, :]), 0.0)
    row_packed = pack_hub(
        row_local_max,
        jnp.sum(row_local_w, 1),
        jnp.einsum("rc,rch->rh", row_local_w, cells_f, precision=HIGH),
        local_row_cot,
    )
    col_packed = pack_hub(
        col_local_max,
        jnp.sum(col_local_w, 0),
        jnp.einsum("rc,rch->ch", col_local_w, cells_f, precision=HIGH),
        local_col_cot,
    )
    row_max, row_total, row_pooled_cells, row_cot = unpack_hub(
        butterfly(row_packed, "col", hub_merge(row_count)), row_count
    )
    col_max, col_total, col_pooled_cells, col_cot = unpack_hub(
        butterfly(col_packed, "row", hub_merge(col_count)), col_count
    )

    row_weights = jnp.where(live_mask, jnp.exp(row_score - row_max[:, None]), 0.0)
    col_weights = jnp.where(live_mask, jnp.exp(col_score - col_max[None, :]), 0.0)
    row_hub = jnp.dot(row_pooled_cells, value_f, precision=HIGH) / row_total[:, None]
    col_hub = jnp.dot(col_pooled_cells, value_f, precision=HIGH) / col_total[:, None]
    out_trans = out_weight.astype(jnp.float32).T
    row_grad = jnp.dot(row_cot, out_trans, precision=HIGH)
    col_grad = jnp.dot(col_cot, out_trans, precision=HIGH)
    row_prob = row_weights / row_total[:, None]
    col_prob = col_weights / col_total[None, :]
    row_dot = jnp.sum(row_hub * row_grad, -1)
    col_dot = jnp.sum(col_hub * col_grad, -1)
    row_grad_cells = jnp.dot(row_grad, value_f.T, precision=HIGH)
    col_grad_cells = jnp.dot(col_grad, value_f.T, precision=HIGH)
    row_dp = jnp.einsum("rch,rh->rc", cells_f, row_grad_cells, precision=HIGH)
    col_dp = jnp.einsum("rch,ch->rc", cells_f, col_grad_cells, precision=HIGH)
    row_ds = row_prob * (row_dp - row_dot[:, None])
    col_ds = col_prob * (col_dp - col_dot[None, :])
    value_grad = (
        row_prob[..., None] * row_grad[:, None, :] + col_prob[..., None] * col_grad[None, :, :]
    ).astype(jnp.bfloat16)
    key_grad = (
        (row_ds[..., None] * row_query + col_ds[..., None] * col_query) * score_scale
    ).astype(jnp.bfloat16)
    row_ds_cells = jnp.einsum("rc,rch->h", row_ds, cells_f, precision=HIGH)
    col_ds_cells = jnp.einsum("rc,rch->h", col_ds, cells_f, precision=HIGH)
    row_query_part = jnp.dot(row_ds_cells, key_f, precision=HIGH) * score_scale
    col_query_part = jnp.dot(col_ds_cells, key_f, precision=HIGH) * score_scale
    flat_cells = cells.reshape(-1, feature_width)
    flat_kg = key_grad.reshape(-1, feature_width)
    flat_vg = value_grad.reshape(-1, feature_width)
    key_part = jnp.einsum("nh,nk->hk", flat_cells, flat_kg, preferred_element_type=jnp.float32)
    value_part = jnp.einsum("nh,nk->hk", flat_cells, flat_vg, preferred_element_type=jnp.float32)
    out_part = jnp.einsum("rh,rk->hk", row_hub, local_row_cot, precision=HIGH)
    out_part = out_part + jnp.einsum("ch,ck->hk", col_hub, local_col_cot, precision=HIGH)
    packed = jnp.concatenate(
        [key_part, value_part, out_part, row_query_part[None], col_query_part[None]], 0
    )
    packed = butterfly(butterfly(packed, "col", jnp.add), "row", jnp.add)
    key_total = packed[:feature_width]
    value_total = packed[feature_width : 2 * feature_width]
    out_total = packed[2 * feature_width : 3 * feature_width]
    row_query_total = packed[3 * feature_width]
    col_query_total = packed[3 * feature_width + 1]
    back = jnp.einsum("nk,hk->nh", flat_kg, key_weight, preferred_element_type=jnp.float32)
    back = back + jnp.einsum("nk,hk->nh", flat_vg, value_weight, preferred_element_type=jnp.float32)
    cell_grad = (upstream_f + back.reshape(cells.shape)).astype(jnp.bfloat16)
    return (cell_grad, key_total, value_total, out_total, row_query_total, col_query_total)


def solution(mesh):
    placed = (P("row", "col", None), P("row", "col", None), P("row"), P(), P(), P(), P(), P())
    return jax.shard_map(
        on_device,
        mesh=mesh,
        in_specs=placed,
        out_specs=(P("row", "col", None), P(), P(), P(), P(), P()),
        check_vma=False,
    )
```

```python
import math

import jax
import jax.numpy as jnp
from jax import lax
from jax.sharding import PartitionSpec as P

NEG_FILL = -1e30
HIGH = lax.Precision.HIGHEST
LANES = 128


def butterfly(state, axis, combine):
    size = lax.axis_size(axis)
    me = lax.axis_index(axis)
    step = 1
    while step < size:
        other = lax.ppermute(state, axis, [(i, i ^ step) for i in range(size)])
        upper = (me & step) != 0
        low = jnp.where(upper, other, state)
        high = jnp.where(upper, state, other)
        state = combine(low, high)
        step *= 2
    return state


def vec_rows(vec):
    pad = (-vec.shape[0]) % LANES
    return jnp.pad(vec, (0, pad)).reshape(-1, LANES)


def pack_hub(local_max, local_total, pooled, cot):
    return jnp.concatenate([pooled, cot, vec_rows(local_max), vec_rows(local_total)], 0)


def unpack_hub(packed, count):
    extra = -(-count // LANES)
    pooled = packed[:count]
    cot = packed[count : 2 * count]
    hub_max = packed[2 * count : 2 * count + extra].reshape(-1)[:count]
    total = packed[2 * count + extra :].reshape(-1)[:count]
    return hub_max, total, pooled, cot


def hub_merge(count):
    def merge(a, b):
        max_a, total_a, pooled_a, cot_a = unpack_hub(a, count)
        max_b, total_b, pooled_b, cot_b = unpack_hub(b, count)
        joint = jnp.maximum(max_a, max_b)
        scale_a = jnp.exp(max_a - joint)
        scale_b = jnp.exp(max_b - joint)
        total = total_a * scale_a + total_b * scale_b
        pooled = pooled_a * scale_a[:, None] + pooled_b * scale_b[:, None]
        return pack_hub(joint, total, pooled, cot_a + cot_b)

    return merge


def scatter_halving(state, axis, combine):
    size = lax.axis_size(axis)
    me = lax.axis_index(axis)
    step = size // 2
    while step >= 1:
        half = state.shape[0] // 2
        upper = (me & step) != 0
        keep = jnp.where(upper, state[half:], state[:half])
        send = jnp.where(upper, state[:half], state[half:])
        other = lax.ppermute(send, axis, [(i, i ^ step) for i in range(size)])
        state = combine(jnp.where(upper, other, keep), jnp.where(upper, keep, other))
        step //= 2
    return state


def gather_doubling(block, axis):
    size = lax.axis_size(axis)
    me = lax.axis_index(axis)
    step = 1
    while step < size:
        other = lax.ppermute(block, axis, [(i, i ^ step) for i in range(size)])
        upper = (me & step) != 0
        block = jnp.where(
            upper, jnp.concatenate([other, block], 0), jnp.concatenate([block, other], 0)
        )
        step *= 2
    return block


def lane_merge(a, b):
    width = LANES
    max_a, max_b = a[:, 2 * width], b[:, 2 * width]
    joint = jnp.maximum(max_a, max_b)
    scale_a = jnp.exp(max_a - joint)[:, None]
    scale_b = jnp.exp(max_b - joint)[:, None]
    pooled = a[:, :width] * scale_a + b[:, :width] * scale_b
    cot = a[:, width : 2 * width] + b[:, width : 2 * width]
    total = a[:, 2 * width + 1 : 2 * width + 2] * scale_a + b[:, 2 * width + 1 : 2 * width + 2] * scale_b
    stats = jnp.concatenate([joint[:, None], total, jnp.zeros_like(a[:, 2 * width + 2 :])], 1)
    return jnp.concatenate([pooled, cot, stats], 1)


def on_device(cells, upstream, counts, key_weight, value_weight, out_weight, row_query, col_query):
    row_count, col_count, feature_width = cells.shape
    score_scale = 1.0 / math.sqrt(feature_width)
    cells_f = cells.astype(jnp.float32)
    upstream_f = upstream.astype(jnp.float32)
    key_f = key_weight.astype(jnp.float32)
    value_f = value_weight.astype(jnp.float32)
    local_row_cot = jnp.sum(upstream_f, 1)
    local_col_cot = jnp.sum(upstream_f, 0)

    row_key_query = jnp.dot(key_f, row_query, precision=HIGH)
    col_key_query = jnp.dot(key_f, col_query, precision=HIGH)
    row_score = jnp.einsum("rch,h->rc", cells_f, row_key_query, precision=HIGH) * score_scale
    col_score = jnp.einsum("rch,h->rc", cells_f, col_key_query, precision=HIGH) * score_scale
    column_ids = lax.axis_index("col") * col_count + jnp.arange(col_count, dtype=jnp.int32)
    live_mask = column_ids[None, :] < counts[:, None]

    row_local_max = jnp.max(jnp.where(live_mask, row_score, NEG_FILL), 1)
    col_local_max = jnp.max(jnp.where(live_mask, col_score, NEG_FILL), 0)
    row_local_w = jnp.where(live_mask, jnp.exp(row_score - row_local_max[:, None]), 0.0)
    col_local_w = jnp.where(live_mask, jnp.exp(col_score - col_local_max[None, :]), 0.0)
    row_packed = pack_hub(
        row_local_max,
        jnp.sum(row_local_w, 1),
        jnp.einsum("rc,rch->rh", row_local_w, cells_f, precision=HIGH),
        local_row_cot,
    )
    col_stats = jnp.zeros((col_count, LANES), jnp.float32)
    col_stats = col_stats.at[:, 0].set(col_local_max).at[:, 1].set(jnp.sum(col_local_w, 0))
    col_packed = jnp.concatenate(
        [
            jnp.einsum("rc,rch->ch", col_local_w, cells_f, precision=HIGH),
            local_col_cot,
            col_stats,
        ],
        1,
    )
    row_max, row_total, row_pooled_cells, row_cot = unpack_hub(
        butterfly(row_packed, "col", hub_merge(row_count)), row_count
    )
    out_trans = out_weight.astype(jnp.float32).T
    own = scatter_halving(col_packed, "row", lane_merge)
    own_total = own[:, 2 * LANES + 1]
    own_hub = jnp.dot(own[:, :LANES], value_f, precision=HIGH) / own_total[:, None]
    own_cot = own[:, LANES : 2 * LANES]
    own_grad = jnp.dot(own_cot, out_trans, precision=HIGH)
    own_dot = jnp.sum(own_hub * own_grad, -1)
    own_out_part = jnp.einsum("ch,ck->hk", own_hub, own_cot, precision=HIGH)
    own_stats = jnp.zeros((own.shape[0], LANES), jnp.float32)
    own_stats = own_stats.at[:, 0].set(own[:, 2 * LANES]).at[:, 1].set(own_total)
    own_stats = own_stats.at[:, 2].set(own_dot)
    col_all = gather_doubling(jnp.concatenate([own_grad, own_stats], 1), "row")
    col_grad = col_all[:, :LANES]
    col_max = col_all[:, LANES]
    col_total = col_all[:, LANES + 1]
    col_dot = col_all[:, LANES + 2]

    row_weights = jnp.where(live_mask, jnp.exp(row_score - row_max[:, None]), 0.0)
    col_weights = jnp.where(live_mask, jnp.exp(col_score - col_max[None, :]), 0.0)
    row_hub = jnp.dot(row_pooled_cells, value_f, precision=HIGH) / row_total[:, None]
    row_grad = jnp.dot(row_cot, out_trans, precision=HIGH)
    row_prob = row_weights / row_total[:, None]
    col_prob = col_weights / col_total[None, :]
    row_dot = jnp.sum(row_hub * row_grad, -1)
    row_grad_cells = jnp.dot(row_grad, value_f.T, precision=HIGH)
    col_grad_cells = jnp.dot(col_grad, value_f.T, precision=HIGH)
    row_dp = jnp.einsum("rch,rh->rc", cells_f, row_grad_cells, precision=HIGH)
    col_dp = jnp.einsum("rch,ch->rc", cells_f, col_grad_cells, precision=HIGH)
    row_ds = row_prob * (row_dp - row_dot[:, None])
    col_ds = col_prob * (col_dp - col_dot[None, :])
    value_grad = (
        row_prob[..., None] * row_grad[:, None, :] + col_prob[..., None] * col_grad[None, :, :]
    ).astype(jnp.bfloat16)
    key_grad = (
        (row_ds[..., None] * row_query + col_ds[..., None] * col_query) * score_scale
    ).astype(jnp.bfloat16)
    row_ds_cells = jnp.einsum("rc,rch->h", row_ds, cells_f, precision=HIGH)
    col_ds_cells = jnp.einsum("rc,rch->h", col_ds, cells_f, precision=HIGH)
    row_query_part = jnp.dot(row_ds_cells, key_f, precision=HIGH) * score_scale
    col_query_part = jnp.dot(col_ds_cells, key_f, precision=HIGH) * score_scale
    flat_cells = cells.reshape(-1, feature_width)
    flat_kg = key_grad.reshape(-1, feature_width)
    flat_vg = value_grad.reshape(-1, feature_width)
    key_part = jnp.einsum("nh,nk->hk", flat_cells, flat_kg, preferred_element_type=jnp.float32)
    value_part = jnp.einsum("nh,nk->hk", flat_cells, flat_vg, preferred_element_type=jnp.float32)
    out_part = jnp.einsum("rh,rk->hk", row_hub, local_row_cot, precision=HIGH)
    out_part = out_part + own_out_part
    packed = jnp.concatenate(
        [key_part, value_part, out_part, row_query_part[None], col_query_part[None]], 0
    )
    packed = butterfly(butterfly(packed, "col", jnp.add), "row", jnp.add)
    key_total = packed[:feature_width]
    value_total = packed[feature_width : 2 * feature_width]
    out_total = packed[2 * feature_width : 3 * feature_width]
    row_query_total = packed[3 * feature_width]
    col_query_total = packed[3 * feature_width + 1]
    back = jnp.einsum("nk,hk->nh", flat_kg, key_weight, preferred_element_type=jnp.float32)
    back = back + jnp.einsum("nk,hk->nh", flat_vg, value_weight, preferred_element_type=jnp.float32)
    cell_grad = (upstream_f + back.reshape(cells.shape)).astype(jnp.bfloat16)
    return (cell_grad, key_total, value_total, out_total, row_query_total, col_query_total)


def solution(mesh):
    placed = (P("row", "col", None), P("row", "col", None), P("row"), P(), P(), P(), P(), P())
    return jax.shard_map(
        on_device,
        mesh=mesh,
        in_specs=placed,
        out_specs=(P("row", "col", None), P(), P(), P(), P(), P()),
        check_vma=False,
    )
```

```python
import math

import jax
import jax.numpy as jnp
from jax import lax
from jax.sharding import PartitionSpec as P

NEG_FILL = -1e30
HIGH = lax.Precision.HIGHEST
LANES = 128


def butterfly(state, axis, combine):
    size = lax.axis_size(axis)
    me = lax.axis_index(axis)
    step = 1
    while step < size:
        other = lax.ppermute(state, axis, [(i, i ^ step) for i in range(size)])
        upper = (me & step) != 0
        low = jnp.where(upper, other, state)
        high = jnp.where(upper, state, other)
        state = combine(low, high)
        step *= 2
    return state


def vec_rows(vec):
    pad = (-vec.shape[0]) % LANES
    return jnp.pad(vec, (0, pad)).reshape(-1, LANES)


def pack_hub(local_max, local_total, pooled, cot):
    return jnp.concatenate([pooled, cot, vec_rows(local_max), vec_rows(local_total)], 0)


def unpack_hub(packed, count):
    extra = -(-count // LANES)
    pooled = packed[:count]
    cot = packed[count : 2 * count]
    hub_max = packed[2 * count : 2 * count + extra].reshape(-1)[:count]
    total = packed[2 * count + extra :].reshape(-1)[:count]
    return hub_max, total, pooled, cot


def hub_merge(count):
    def merge(a, b):
        max_a, total_a, pooled_a, cot_a = unpack_hub(a, count)
        max_b, total_b, pooled_b, cot_b = unpack_hub(b, count)
        joint = jnp.maximum(max_a, max_b)
        scale_a = jnp.exp(max_a - joint)
        scale_b = jnp.exp(max_b - joint)
        total = total_a * scale_a + total_b * scale_b
        pooled = pooled_a * scale_a[:, None] + pooled_b * scale_b[:, None]
        return pack_hub(joint, total, pooled, cot_a + cot_b)

    return merge


def scatter_halving(state, axis, combine):
    size = lax.axis_size(axis)
    me = lax.axis_index(axis)
    step = size // 2
    while step >= 1:
        half = state.shape[0] // 2
        upper = (me & step) != 0
        keep = jnp.where(upper, state[half:], state[:half])
        send = jnp.where(upper, state[:half], state[half:])
        other = lax.ppermute(send, axis, [(i, i ^ step) for i in range(size)])
        state = combine(jnp.where(upper, other, keep), jnp.where(upper, keep, other))
        step //= 2
    return state


def gather_doubling(block, axis):
    size = lax.axis_size(axis)
    me = lax.axis_index(axis)
    step = 1
    while step < size:
        other = lax.ppermute(block, axis, [(i, i ^ step) for i in range(size)])
        upper = (me & step) != 0
        block = jnp.where(
            upper, jnp.concatenate([other, block], 0), jnp.concatenate([block, other], 0)
        )
        step *= 2
    return block


def lane_merge(a, b):
    width = LANES
    max_a, max_b = a[:, 2 * width], b[:, 2 * width]
    joint = jnp.maximum(max_a, max_b)
    scale_a = jnp.exp(max_a - joint)[:, None]
    scale_b = jnp.exp(max_b - joint)[:, None]
    pooled = a[:, :width] * scale_a + b[:, :width] * scale_b
    cot = a[:, width : 2 * width] + b[:, width : 2 * width]
    total = a[:, 2 * width + 1 : 2 * width + 2] * scale_a + b[:, 2 * width + 1 : 2 * width + 2] * scale_b
    stats = jnp.concatenate([joint[:, None], total, jnp.zeros_like(a[:, 2 * width + 2 :])], 1)
    return jnp.concatenate([pooled, cot, stats], 1)


def on_device(cells, upstream, counts, key_weight, value_weight, out_weight, row_query, col_query):
    row_count, col_count, feature_width = cells.shape
    score_scale = 1.0 / math.sqrt(feature_width)
    cells_f = cells.astype(jnp.float32)
    upstream_f = upstream.astype(jnp.float32)
    key_f = key_weight.astype(jnp.float32)
    value_f = value_weight.astype(jnp.float32)
    local_row_cot = jnp.sum(upstream_f, 1)
    local_col_cot = jnp.sum(upstream_f, 0)

    row_key_query = jnp.dot(key_f, row_query, precision=HIGH)
    col_key_query = jnp.dot(key_f, col_query, precision=HIGH)
    row_score = jnp.einsum("rch,h->rc", cells_f, row_key_query, precision=HIGH) * score_scale
    col_score = jnp.einsum("rch,h->rc", cells_f, col_key_query, precision=HIGH) * score_scale
    column_ids = lax.axis_index("col") * col_count + jnp.arange(col_count, dtype=jnp.int32)
    live_mask = column_ids[None, :] < counts[:, None]

    row_local_max = jnp.max(jnp.where(live_mask, row_score, NEG_FILL), 1)
    col_local_max = jnp.max(jnp.where(live_mask, col_score, NEG_FILL), 0)
    row_local_w = jnp.where(live_mask, jnp.exp(row_score - row_local_max[:, None]), 0.0)
    col_local_w = jnp.where(live_mask, jnp.exp(col_score - col_local_max[None, :]), 0.0)
    row_packed = pack_hub(
        row_local_max,
        jnp.sum(row_local_w, 1),
        jnp.einsum("rc,rch->rh", row_local_w, cells_f, precision=HIGH),
        local_row_cot,
    )
    col_stats = jnp.zeros((col_count, LANES), jnp.float32)
    col_stats = col_stats.at[:, 0].set(col_local_max).at[:, 1].set(jnp.sum(col_local_w, 0))
    col_packed = jnp.concatenate(
        [
            jnp.einsum("rc,rch->ch", col_local_w, cells_f, precision=HIGH),
            local_col_cot,
            col_stats,
        ],
        1,
    )
    row_packed, col_packed = lax.optimization_barrier((row_packed, col_packed))
    row_max, row_total, row_pooled_cells, row_cot = unpack_hub(
        butterfly(row_packed, "col", hub_merge(row_count)), row_count
    )
    out_trans = out_weight.astype(jnp.float32).T
    own = scatter_halving(col_packed, "row", lane_merge)
    own_total = own[:, 2 * LANES + 1]
    own_hub = jnp.dot(own[:, :LANES], value_f, precision=HIGH) / own_total[:, None]
    own_cot = own[:, LANES : 2 * LANES]
    own_grad = jnp.dot(own_cot, out_trans, precision=HIGH)
    own_dot = jnp.sum(own_hub * own_grad, -1)
    own_out_part = jnp.einsum("ch,ck->hk", own_hub, own_cot, precision=HIGH)
    own_stats = jnp.zeros((own.shape[0], LANES), jnp.float32)
    own_stats = own_stats.at[:, 0].set(own[:, 2 * LANES]).at[:, 1].set(own_total)
    own_stats = own_stats.at[:, 2].set(own_dot)
    col_all = gather_doubling(jnp.concatenate([own_grad, own_stats], 1), "row")
    col_grad = col_all[:, :LANES]
    col_max = col_all[:, LANES]
    col_total = col_all[:, LANES + 1]
    col_dot = col_all[:, LANES + 2]

    row_weights = jnp.where(live_mask, jnp.exp(row_score - row_max[:, None]), 0.0)
    col_weights = jnp.where(live_mask, jnp.exp(col_score - col_max[None, :]), 0.0)
    row_hub = jnp.dot(row_pooled_cells, value_f, precision=HIGH) / row_total[:, None]
    row_grad = jnp.dot(row_cot, out_trans, precision=HIGH)
    row_prob = row_weights / row_total[:, None]
    col_prob = col_weights / col_total[None, :]
    row_dot = jnp.sum(row_hub * row_grad, -1)
    row_grad_cells = jnp.dot(row_grad, value_f.T, precision=HIGH)
    col_grad_cells = jnp.dot(col_grad, value_f.T, precision=HIGH)
    row_dp = jnp.einsum("rch,rh->rc", cells_f, row_grad_cells, precision=HIGH)
    col_dp = jnp.einsum("rch,ch->rc", cells_f, col_grad_cells, precision=HIGH)
    row_ds = row_prob * (row_dp - row_dot[:, None])
    col_ds = col_prob * (col_dp - col_dot[None, :])
    value_grad = (
        row_prob[..., None] * row_grad[:, None, :] + col_prob[..., None] * col_grad[None, :, :]
    ).astype(jnp.bfloat16)
    key_grad = (
        (row_ds[..., None] * row_query + col_ds[..., None] * col_query) * score_scale
    ).astype(jnp.bfloat16)
    row_ds_cells = jnp.einsum("rc,rch->h", row_ds, cells_f, precision=HIGH)
    col_ds_cells = jnp.einsum("rc,rch->h", col_ds, cells_f, precision=HIGH)
    row_query_part = jnp.dot(row_ds_cells, key_f, precision=HIGH) * score_scale
    col_query_part = jnp.dot(col_ds_cells, key_f, precision=HIGH) * score_scale
    flat_cells = cells.reshape(-1, feature_width)
    flat_kg = key_grad.reshape(-1, feature_width)
    flat_vg = value_grad.reshape(-1, feature_width)
    key_part = jnp.einsum("nh,nk->hk", flat_cells, flat_kg, preferred_element_type=jnp.float32)
    value_part = jnp.einsum("nh,nk->hk", flat_cells, flat_vg, preferred_element_type=jnp.float32)
    out_part = jnp.einsum("rh,rk->hk", row_hub, local_row_cot, precision=HIGH)
    out_part = out_part + own_out_part
    packed = jnp.concatenate(
        [key_part, value_part, out_part, row_query_part[None], col_query_part[None]], 0
    )
    packed = butterfly(butterfly(packed, "col", jnp.add), "row", jnp.add)
    key_total = packed[:feature_width]
    value_total = packed[feature_width : 2 * feature_width]
    out_total = packed[2 * feature_width : 3 * feature_width]
    row_query_total = packed[3 * feature_width]
    col_query_total = packed[3 * feature_width + 1]
    back = jnp.einsum("nk,hk->nh", flat_kg, key_weight, preferred_element_type=jnp.float32)
    back = back + jnp.einsum("nk,hk->nh", flat_vg, value_weight, preferred_element_type=jnp.float32)
    cell_grad = (upstream_f + back.reshape(cells.shape)).astype(jnp.bfloat16)
    return (cell_grad, key_total, value_total, out_total, row_query_total, col_query_total)


def solution(mesh):
    placed = (P("row", "col", None), P("row", "col", None), P("row"), P(), P(), P(), P(), P())
    return jax.shard_map(
        on_device,
        mesh=mesh,
        in_specs=placed,
        out_specs=(P("row", "col", None), P(), P(), P(), P(), P()),
        check_vma=False,
    )
```

```python
import math

import jax
import jax.numpy as jnp
from jax import lax
from jax.sharding import PartitionSpec as P

NEG_FILL = -1e30
HIGH = lax.Precision.HIGHEST
LANES = 128


def butterfly(state, axis, combine):
    size = lax.axis_size(axis)
    me = lax.axis_index(axis)
    step = 1
    while step < size:
        other = lax.ppermute(state, axis, [(i, i ^ step) for i in range(size)])
        upper = (me & step) != 0
        low = jnp.where(upper, other, state)
        high = jnp.where(upper, state, other)
        state = combine(low, high)
        step *= 2
    return state


def vec_rows(vec):
    pad = (-vec.shape[0]) % LANES
    return jnp.pad(vec, (0, pad)).reshape(-1, LANES)


def pack_hub(local_max, local_total, pooled, cot):
    return jnp.concatenate([pooled, cot, vec_rows(local_max), vec_rows(local_total)], 0)


def unpack_hub(packed, count):
    extra = -(-count // LANES)
    pooled = packed[:count]
    cot = packed[count : 2 * count]
    hub_max = packed[2 * count : 2 * count + extra].reshape(-1)[:count]
    total = packed[2 * count + extra :].reshape(-1)[:count]
    return hub_max, total, pooled, cot


def hub_merge(count):
    def merge(a, b):
        max_a, total_a, pooled_a, cot_a = unpack_hub(a, count)
        max_b, total_b, pooled_b, cot_b = unpack_hub(b, count)
        joint = jnp.maximum(max_a, max_b)
        scale_a = jnp.exp(max_a - joint)
        scale_b = jnp.exp(max_b - joint)
        total = total_a * scale_a + total_b * scale_b
        pooled = pooled_a * scale_a[:, None] + pooled_b * scale_b[:, None]
        return pack_hub(joint, total, pooled, cot_a + cot_b)

    return merge


def scatter_halving(state, axis, combine):
    size = lax.axis_size(axis)
    me = lax.axis_index(axis)
    step = size // 2
    while step >= 1:
        half = state.shape[0] // 2
        upper = (me & step) != 0
        keep = jnp.where(upper, state[half:], state[:half])
        send = jnp.where(upper, state[:half], state[half:])
        other = lax.ppermute(send, axis, [(i, i ^ step) for i in range(size)])
        state = combine(jnp.where(upper, other, keep), jnp.where(upper, keep, other))
        step //= 2
    return state


def gather_doubling(block, axis):
    size = lax.axis_size(axis)
    me = lax.axis_index(axis)
    step = 1
    while step < size:
        other = lax.ppermute(block, axis, [(i, i ^ step) for i in range(size)])
        upper = (me & step) != 0
        block = jnp.where(
            upper, jnp.concatenate([other, block], 0), jnp.concatenate([block, other], 0)
        )
        step *= 2
    return block


def lane_merge(a, b):
    width = LANES
    max_a, max_b = a[:, 2 * width], b[:, 2 * width]
    joint = jnp.maximum(max_a, max_b)
    scale_a = jnp.exp(max_a - joint)[:, None]
    scale_b = jnp.exp(max_b - joint)[:, None]
    pooled = a[:, :width] * scale_a + b[:, :width] * scale_b
    cot = a[:, width : 2 * width] + b[:, width : 2 * width]
    total = a[:, 2 * width + 1 : 2 * width + 2] * scale_a + b[:, 2 * width + 1 : 2 * width + 2] * scale_b
    stats = jnp.concatenate([joint[:, None], total, jnp.zeros_like(a[:, 2 * width + 2 :])], 1)
    return jnp.concatenate([pooled, cot, stats], 1)


def on_device(cells, upstream, counts, key_weight, value_weight, out_weight, row_query, col_query):
    row_count, col_count, feature_width = cells.shape
    score_scale = 1.0 / math.sqrt(feature_width)
    cells_f = cells.astype(jnp.float32)
    upstream_f = upstream.astype(jnp.float32)
    key_f = key_weight.astype(jnp.float32)
    value_f = value_weight.astype(jnp.float32)
    local_row_cot = jnp.sum(upstream_f, 1)
    local_col_cot = jnp.sum(upstream_f, 0)

    row_key_query = jnp.dot(key_f, row_query, precision=HIGH)
    col_key_query = jnp.dot(key_f, col_query, precision=HIGH)
    row_score = jnp.sum(cells_f * row_key_query, -1) * score_scale
    col_score = jnp.sum(cells_f * col_key_query, -1) * score_scale
    column_ids = lax.axis_index("col") * col_count + jnp.arange(col_count, dtype=jnp.int32)
    live_mask = column_ids[None, :] < counts[:, None]

    row_local_max = jnp.max(jnp.where(live_mask, row_score, NEG_FILL), 1)
    col_local_max = jnp.max(jnp.where(live_mask, col_score, NEG_FILL), 0)
    row_local_w = jnp.where(live_mask, jnp.exp(row_score - row_local_max[:, None]), 0.0)
    col_local_w = jnp.where(live_mask, jnp.exp(col_score - col_local_max[None, :]), 0.0)
    row_packed = pack_hub(
        row_local_max,
        jnp.sum(row_local_w, 1),
        jnp.sum(row_local_w[..., None] * cells_f, 1),
        local_row_cot,
    )
    col_stats = jnp.zeros((col_count, LANES), jnp.float32)
    col_stats = col_stats.at[:, 0].set(col_local_max).at[:, 1].set(jnp.sum(col_local_w, 0))
    col_packed = jnp.concatenate(
        [
            jnp.sum(col_local_w[..., None] * cells_f, 0),
            local_col_cot,
            col_stats,
        ],
        1,
    )
    row_packed, col_packed = lax.optimization_barrier((row_packed, col_packed))
    row_max, row_total, row_pooled_cells, row_cot = unpack_hub(
        butterfly(row_packed, "col", hub_merge(row_count)), row_count
    )
    out_trans = out_weight.astype(jnp.float32).T
    own = scatter_halving(col_packed, "row", lane_merge)
    own_total = own[:, 2 * LANES + 1]
    own_hub = jnp.dot(own[:, :LANES], value_f, precision=HIGH) / own_total[:, None]
    own_cot = own[:, LANES : 2 * LANES]
    own_grad = jnp.dot(own_cot, out_trans, precision=HIGH)
    own_dot = jnp.sum(own_hub * own_grad, -1)
    own_out_part = jnp.einsum("ch,ck->hk", own_hub, own_cot, precision=HIGH)
    own_stats = jnp.zeros((own.shape[0], LANES), jnp.float32)
    own_stats = own_stats.at[:, 0].set(own[:, 2 * LANES]).at[:, 1].set(own_total)
    own_stats = own_stats.at[:, 2].set(own_dot)
    col_all = gather_doubling(jnp.concatenate([own_grad, own_stats], 1), "row")
    col_grad = col_all[:, :LANES]
    col_max = col_all[:, LANES]
    col_total = col_all[:, LANES + 1]
    col_dot = col_all[:, LANES + 2]

    row_weights = jnp.where(live_mask, jnp.exp(row_score - row_max[:, None]), 0.0)
    col_weights = jnp.where(live_mask, jnp.exp(col_score - col_max[None, :]), 0.0)
    row_hub = jnp.dot(row_pooled_cells, value_f, precision=HIGH) / row_total[:, None]
    row_grad = jnp.dot(row_cot, out_trans, precision=HIGH)
    row_prob = row_weights / row_total[:, None]
    col_prob = col_weights / col_total[None, :]
    row_dot = jnp.sum(row_hub * row_grad, -1)
    row_grad_cells = jnp.dot(row_grad, value_f.T, precision=HIGH)
    col_grad_cells = jnp.dot(col_grad, value_f.T, precision=HIGH)
    row_dp = jnp.sum(cells_f * row_grad_cells[:, None, :], -1)
    col_dp = jnp.sum(cells_f * col_grad_cells[None, :, :], -1)
    row_ds = row_prob * (row_dp - row_dot[:, None])
    col_ds = col_prob * (col_dp - col_dot[None, :])
    value_grad = (
        row_prob[..., None] * row_grad[:, None, :] + col_prob[..., None] * col_grad[None, :, :]
    ).astype(jnp.bfloat16)
    key_grad = (
        (row_ds[..., None] * row_query + col_ds[..., None] * col_query) * score_scale
    ).astype(jnp.bfloat16)
    row_ds_cells = jnp.sum(row_ds[..., None] * cells_f, (0, 1))
    col_ds_cells = jnp.sum(col_ds[..., None] * cells_f, (0, 1))
    row_query_part = jnp.dot(row_ds_cells, key_f, precision=HIGH) * score_scale
    col_query_part = jnp.dot(col_ds_cells, key_f, precision=HIGH) * score_scale
    flat_cells = cells.reshape(-1, feature_width)
    flat_kg = key_grad.reshape(-1, feature_width)
    flat_vg = value_grad.reshape(-1, feature_width)
    key_part = jnp.einsum("nh,nk->hk", flat_cells, flat_kg, preferred_element_type=jnp.float32)
    value_part = jnp.einsum("nh,nk->hk", flat_cells, flat_vg, preferred_element_type=jnp.float32)
    out_part = jnp.einsum("rh,rk->hk", row_hub, local_row_cot, precision=HIGH)
    out_part = out_part + own_out_part
    packed = jnp.concatenate(
        [key_part, value_part, out_part, row_query_part[None], col_query_part[None]], 0
    )
    packed = butterfly(butterfly(packed, "col", jnp.add), "row", jnp.add)
    key_total = packed[:feature_width]
    value_total = packed[feature_width : 2 * feature_width]
    out_total = packed[2 * feature_width : 3 * feature_width]
    row_query_total = packed[3 * feature_width]
    col_query_total = packed[3 * feature_width + 1]
    back = jnp.einsum("nk,hk->nh", flat_kg, key_weight, preferred_element_type=jnp.float32)
    back = back + jnp.einsum("nk,hk->nh", flat_vg, value_weight, preferred_element_type=jnp.float32)
    cell_grad = (upstream_f + back.reshape(cells.shape)).astype(jnp.bfloat16)
    return (cell_grad, key_total, value_total, out_total, row_query_total, col_query_total)


def solution(mesh):
    placed = (P("row", "col", None), P("row", "col", None), P("row"), P(), P(), P(), P(), P())
    return jax.shard_map(
        on_device,
        mesh=mesh,
        in_specs=placed,
        out_specs=(P("row", "col", None), P(), P(), P(), P(), P()),
        check_vma=False,
    )
```

```python
import math

import jax
import jax.numpy as jnp
from jax import lax
from jax.sharding import PartitionSpec as P

NEG_FILL = -1e30
HIGH = lax.Precision.HIGHEST
LANES = 128


def butterfly(state, axis, combine):
    size = lax.axis_size(axis)
    me = lax.axis_index(axis)
    step = 1
    while step < size:
        other = lax.ppermute(state, axis, [(i, i ^ step) for i in range(size)])
        upper = (me & step) != 0
        low = jnp.where(upper, other, state)
        high = jnp.where(upper, state, other)
        state = combine(low, high)
        step *= 2
    return state


def vec_rows(vec):
    pad = (-vec.shape[0]) % LANES
    return jnp.pad(vec, (0, pad)).reshape(-1, LANES)


def pack_hub(local_max, local_total, pooled, cot):
    return jnp.concatenate([pooled, cot, vec_rows(local_max), vec_rows(local_total)], 0)


def unpack_hub(packed, count):
    extra = -(-count // LANES)
    pooled = packed[:count]
    cot = packed[count : 2 * count]
    hub_max = packed[2 * count : 2 * count + extra].reshape(-1)[:count]
    total = packed[2 * count + extra :].reshape(-1)[:count]
    return hub_max, total, pooled, cot


def hub_merge(count):
    def merge(a, b):
        max_a, total_a, pooled_a, cot_a = unpack_hub(a, count)
        max_b, total_b, pooled_b, cot_b = unpack_hub(b, count)
        joint = jnp.maximum(max_a, max_b)
        scale_a = jnp.exp(max_a - joint)
        scale_b = jnp.exp(max_b - joint)
        total = total_a * scale_a + total_b * scale_b
        pooled = pooled_a * scale_a[:, None] + pooled_b * scale_b[:, None]
        return pack_hub(joint, total, pooled, cot_a + cot_b)

    return merge


def scatter_halving(state, axis, combine):
    size = lax.axis_size(axis)
    me = lax.axis_index(axis)
    step = size // 2
    while step >= 1:
        half = state.shape[0] // 2
        upper = (me & step) != 0
        keep = jnp.where(upper, state[half:], state[:half])
        send = jnp.where(upper, state[:half], state[half:])
        other = lax.ppermute(send, axis, [(i, i ^ step) for i in range(size)])
        state = combine(jnp.where(upper, other, keep), jnp.where(upper, keep, other))
        step //= 2
    return state


def gather_doubling(block, axis):
    size = lax.axis_size(axis)
    me = lax.axis_index(axis)
    step = 1
    while step < size:
        other = lax.ppermute(block, axis, [(i, i ^ step) for i in range(size)])
        upper = (me & step) != 0
        block = jnp.where(
            upper, jnp.concatenate([other, block], 0), jnp.concatenate([block, other], 0)
        )
        step *= 2
    return block


def lane_merge(a, b):
    width = LANES
    max_a, max_b = a[:, 2 * width], b[:, 2 * width]
    joint = jnp.maximum(max_a, max_b)
    scale_a = jnp.exp(max_a - joint)[:, None]
    scale_b = jnp.exp(max_b - joint)[:, None]
    pooled = a[:, :width] * scale_a + b[:, :width] * scale_b
    cot = a[:, width : 2 * width] + b[:, width : 2 * width]
    total = a[:, 2 * width + 1 : 2 * width + 2] * scale_a + b[:, 2 * width + 1 : 2 * width + 2] * scale_b
    stats = jnp.concatenate([joint[:, None], total, jnp.zeros_like(a[:, 2 * width + 2 :])], 1)
    return jnp.concatenate([pooled, cot, stats], 1)


def on_device(cells, upstream, counts, key_weight, value_weight, out_weight, row_query, col_query):
    row_count, col_count, feature_width = cells.shape
    score_scale = 1.0 / math.sqrt(feature_width)
    cells_f = cells.astype(jnp.float32)
    upstream_f = upstream.astype(jnp.float32)
    key_f = key_weight.astype(jnp.float32)
    value_f = value_weight.astype(jnp.float32)
    local_row_cot = jnp.sum(upstream_f, 1)
    local_col_cot = jnp.sum(upstream_f, 0)

    row_key_query = jnp.dot(key_f, row_query, precision=HIGH)
    col_key_query = jnp.dot(key_f, col_query, precision=HIGH)
    row_score = jnp.sum(cells_f * row_key_query, -1) * score_scale
    col_score = jnp.sum(cells_f * col_key_query, -1) * score_scale
    column_ids = lax.axis_index("col") * col_count + jnp.arange(col_count, dtype=jnp.int32)
    live_mask = column_ids[None, :] < counts[:, None]

    row_local_max = jnp.max(jnp.where(live_mask, row_score, NEG_FILL), 1)
    col_local_max = jnp.max(jnp.where(live_mask, col_score, NEG_FILL), 0)
    row_local_w = jnp.where(live_mask, jnp.exp(row_score - row_local_max[:, None]), 0.0)
    col_local_w = jnp.where(live_mask, jnp.exp(col_score - col_local_max[None, :]), 0.0)
    row_packed = pack_hub(
        row_local_max,
        jnp.sum(row_local_w, 1),
        jnp.sum(row_local_w[..., None] * cells_f, 1),
        local_row_cot,
    )
    col_stats = jnp.zeros((col_count, LANES), jnp.float32)
    col_stats = col_stats.at[:, 0].set(col_local_max).at[:, 1].set(jnp.sum(col_local_w, 0))
    col_packed = jnp.concatenate(
        [
            jnp.sum(col_local_w[..., None] * cells_f, 0),
            local_col_cot,
            col_stats,
        ],
        1,
    )
    row_packed, col_packed = lax.optimization_barrier((row_packed, col_packed))
    row_max, row_total, row_pooled_cells, row_cot = unpack_hub(
        butterfly(row_packed, "col", hub_merge(row_count)), row_count
    )
    out_trans = out_weight.astype(jnp.float32).T
    own = scatter_halving(col_packed, "row", lane_merge)
    own_total = own[:, 2 * LANES + 1]
    own_hub = jnp.dot(own[:, :LANES], value_f, precision=HIGH) / own_total[:, None]
    own_cot = own[:, LANES : 2 * LANES]
    own_grad = jnp.dot(own_cot, out_trans, precision=HIGH)
    own_dot = jnp.sum(own_hub * own_grad, -1)
    own_stats = jnp.zeros((own.shape[0], LANES), jnp.float32)
    own_stats = own_stats.at[:, 0].set(own[:, 2 * LANES]).at[:, 1].set(own_total)
    own_stats = own_stats.at[:, 2].set(own_dot)
    col_all = gather_doubling(jnp.concatenate([own_grad, own_stats], 1), "row")
    col_grad = col_all[:, :LANES]
    col_max = col_all[:, LANES]
    col_total = col_all[:, LANES + 1]
    col_dot = col_all[:, LANES + 2]

    row_weights = jnp.where(live_mask, jnp.exp(row_score - row_max[:, None]), 0.0)
    col_weights = jnp.where(live_mask, jnp.exp(col_score - col_max[None, :]), 0.0)
    row_hub = jnp.dot(row_pooled_cells, value_f, precision=HIGH) / row_total[:, None]
    row_grad = jnp.dot(row_cot, out_trans, precision=HIGH)
    row_prob = row_weights / row_total[:, None]
    col_prob = col_weights / col_total[None, :]
    row_dot = jnp.sum(row_hub * row_grad, -1)
    row_grad_cells = jnp.dot(row_grad, value_f.T, precision=HIGH)
    col_grad_cells = jnp.dot(col_grad, value_f.T, precision=HIGH)
    row_dp = jnp.sum(cells_f * row_grad_cells[:, None, :], -1)
    col_dp = jnp.sum(cells_f * col_grad_cells[None, :, :], -1)
    row_ds = row_prob * (row_dp - row_dot[:, None])
    col_ds = col_prob * (col_dp - col_dot[None, :])
    value_grad = (
        row_prob[..., None] * row_grad[:, None, :] + col_prob[..., None] * col_grad[None, :, :]
    ).astype(jnp.bfloat16)
    key_grad = (
        (row_ds[..., None] * row_query + col_ds[..., None] * col_query) * score_scale
    ).astype(jnp.bfloat16)
    row_ds_cells = jnp.sum(row_ds[..., None] * cells_f, (0, 1))
    col_ds_cells = jnp.sum(col_ds[..., None] * cells_f, (0, 1))
    flat_kg = key_grad.reshape(-1, feature_width)
    flat_vg = value_grad.reshape(-1, feature_width)
    first_col = (lax.axis_index("col") == 0).astype(jnp.float32)
    row_norm = row_pooled_cells / row_total[:, None]
    own_norm = own[:, :LANES] / own_total[:, None]
    hub_moment = jnp.einsum("rh,rk->hk", row_norm, row_cot, precision=HIGH) * first_col
    hub_moment = hub_moment + jnp.einsum("ch,ck->hk", own_norm, own_cot, precision=HIGH)
    packed = jnp.concatenate([hub_moment, row_ds_cells[None], col_ds_cells[None]], 0)
    packed = butterfly(butterfly(packed, "col", jnp.add), "row", jnp.add)
    moment_total = packed[:feature_width]
    row_ds_total = packed[feature_width]
    col_ds_total = packed[feature_width + 1]
    key_total = (
        row_ds_total[:, None] * row_query[None, :] + col_ds_total[:, None] * col_query[None, :]
    ) * score_scale
    value_total = jnp.dot(moment_total, out_trans, precision=HIGH)
    out_total = jnp.dot(value_f.T, moment_total, precision=HIGH)
    row_query_total = jnp.dot(row_ds_total, key_f, precision=HIGH) * score_scale
    col_query_total = jnp.dot(col_ds_total, key_f, precision=HIGH) * score_scale
    back = jnp.einsum("nk,hk->nh", flat_kg, key_weight, preferred_element_type=jnp.float32)
    back = back + jnp.einsum("nk,hk->nh", flat_vg, value_weight, preferred_element_type=jnp.float32)
    cell_grad = (upstream_f + back.reshape(cells.shape)).astype(jnp.bfloat16)
    return (cell_grad, key_total, value_total, out_total, row_query_total, col_query_total)


def solution(mesh):
    placed = (P("row", "col", None), P("row", "col", None), P("row"), P(), P(), P(), P(), P())
    return jax.shard_map(
        on_device,
        mesh=mesh,
        in_specs=placed,
        out_specs=(P("row", "col", None), P(), P(), P(), P(), P()),
        check_vma=False,
    )
```
